256 devices in a mesh: tm: 2 (over core), scen: 4 (over x), line: 32 (over z, y).
Axes of the slice: x: 4, y: 4, z: 8, core: 2. Of those that a mesh axis runs over, the one named last changes fastest.
Arguments:
- line_blocks: bfloat16 [64, 128, 1024], P('line'), may hold values from -0.1875 to 0.1875
- binding: int32 [128, 2, 8], P(('scen', 'line'), 'tm'), may hold values from 0 to 63, as said below
- line_weight: float32 [128, 2, 8, 128], P(('scen', 'line'), 'tm'), may hold values from 0.25 to 4
- barrier: float32 [128, 2, 1024], P(('scen', 'line'), 'tm'), may hold values from 0.5 to 4
- gradient: float32 [128, 2, 1024], P(('scen', 'line'), 'tm'), may hold values from -6 to 6
- link_columns: bfloat16 [128, 2, 1024, 128], P(('scen', 'line'), 'tm'), may hold values from -0.5 to 0.5
- ramp_weight: float32 [256], replicated, may hold values from 10 to 200
- link_diag: float32 [128], replicated, may hold values from 0.5 to 5
- link_rhs: float32 [128], replicated, may hold values from -18 to 18
Outputs:
- newton_step: float32 [128, 2, 1024], P(('scen', 'line'), 'tm')
- link_step: float32 [128], replicated
The draws below stay inside these ranges and needn't reach their ends.
Inputs may be any that keep to these rules, and one draw needn't show every extreme that they name: Block numbers b are held by line device b // 2. Take the list binding[s, t] of one scenario s and period t: exactly one line device holds 2 of its blocks, no line device holds more, and the other blocks are spread as evenly as possible over the other line devices, in a shuffled order. A block may appear more than once.
All inputs are finite; a program needn't handle non-finite values.
Results may differ from the reference program's by a relative error of at most 0.00084.
Values may be sent and summed in bfloat16 or wider, within the bound.
No kernel may reach another device: no remote copies, remote signals or barrier semaphores. Data moves between devices by JAX's collectives and lax.ppermute only.
A program may use at most 128 MiB of HBM per device.

```python
import math
import jax
import jax.numpy as jnp
from jax import lax

K = 1024
G = 256
L = 128
PB = 128
NBIND = 8
NB_DEV = 2
TPD = 1
PER = 2
SCEN = 128
NB = 64
MOST = 2


def draw_binding(key, part):
    owners = NB // NB_DEV
    shard_count = PER // TPD
    group_count = SCEN * shard_count
    group_slots = TPD * NBIND
    group_keys = jax.random.split(key, group_count)

    def one_group(group_key):
        key_owner, key_local, key_order = jax.random.split(group_key, 3)
        owner_order = jax.random.permutation(key_owner, owners)
        slots = jnp.arange(group_slots, dtype=jnp.int32)
        spread = 1 + jnp.maximum(slots - MOST, 0) % (owners - 1)
        chosen = jnp.where(slots < MOST, 0, spread)
        owner_of = owner_order[chosen]
        local_index = jax.random.randint(key_local, (group_slots,), 0, NB_DEV)
        blocks = owner_of * NB_DEV + local_index
        return blocks[jax.random.permutation(key_order, group_slots)]
    return jax.vmap(one_group)(group_keys).reshape(SCEN, PER, NBIND).astype(jnp.int32)


def steps_of(key, shape, cuts, least, top_value):
    factor_of = 1.0
    for position, parts in cuts:
        steps = jax.random.uniform(jax.random.fold_in(jax.random.fold_in(key, 6), position), (parts,), jnp.float32, least / len(cuts), top_value / len(cuts))
        factor_of = factor_of * jnp.repeat(jnp.exp(steps), shape[position] // parts).reshape((-1,) + (1,) * (len(shape) - 1 - position))
    return factor_of


def normal_values(key, extent, width, bound, cuts=(), kind=jnp.bfloat16):
    values = width * jax.random.normal(key, extent, jnp.float32)
    if cuts:
        values = values * steps_of(key, extent, cuts, -0.22, 0.18)
    return jnp.clip(values, -bound, bound).astype(kind)


def setup_inputs(seed: int = 0) -> dict:
    keys = jax.random.split(jax.random.key(seed), 10)
    return {
        "line_blocks": normal_values(keys[0], (NB, PB, K), K ** -0.5, 0.1875, ((0, 32),)),
        "binding": draw_binding(jax.random.fold_in(keys[9], 71), 0),
        "line_weight": jnp.clip(jnp.exp(math.log(4.0) - 2.7725887 * jax.random.uniform(keys[2], (SCEN, PER, NBIND, PB), jnp.float32) ** steps_of(keys[2], (SCEN, PER, NBIND, PB), ((0, 128), (1, 2)), -0.2, 0.2)), 0.25, 4.0),
        "barrier": jnp.clip(jnp.exp(math.log(4.0) - 2.0794415 * jax.random.uniform(keys[3], (SCEN, PER, K), jnp.float32) ** steps_of(keys[3], (SCEN, PER, K), ((0, 128), (1, 2)), -0.2, 0.2)), 0.5, 4.0),
        "gradient": normal_values(keys[4], (SCEN, PER, K), 1.0, 6.0, ((0, 128), (1, 2)), jnp.float32),
        "link_columns": normal_values(keys[5], (SCEN, PER, K, L), (K // 9) ** -0.5, 0.5, ((0, 128), (1, 2))),
        "ramp_weight": jnp.clip(jnp.exp(jax.random.uniform(keys[6], (G,), jnp.float32, math.log(10.0), math.log(200.0))), 10.0, 200.0),
        "link_diag": jnp.clip(jnp.exp(jax.random.uniform(keys[7], (L,), jnp.float32, math.log(0.5), math.log(5.0))), 0.5, 5.0),
        "link_rhs": normal_values(keys[8], (L,), 3.0, 18.0, (), jnp.float32),
    }


highest = lax.Precision.HIGHEST

def period_hessian(selected, weights, barrier_row, ramp_weight, end_factor):
    order = selected.shape[-1]
    scaled = (weights[:, :, None] * selected.astype(jnp.float32)).astype(jnp.bfloat16)
    flat = selected.reshape(-1, order)
    scaled_flat = scaled.reshape(-1, order)
    hessian = jnp.dot(flat.T.astype(jnp.float32), scaled_flat.astype(jnp.float32), preferred_element_type=jnp.float32)
    count = ramp_weight.shape[0]
    extra = jnp.concatenate([end_factor * ramp_weight, jnp.zeros((order - count,), jnp.float32)])
    return hessian + jnp.diag(barrier_row + extra)

def eliminate(hessian, grad_row, link_mat, carry, ramp_weight):
    mat_in, vec_in, cols_in = carry
    count = ramp_weight.shape[0]
    schur = hessian.at[:count, :count].add(-mat_in)
    right_vec = grad_row.at[:count].add(vec_in)
    right_mat = link_mat.astype(jnp.float32).at[:count].add(cols_in)
    lower = jnp.linalg.cholesky(schur)
    unit = jnp.eye(hessian.shape[0], count, dtype=jnp.float32)
    solved = jax.scipy.linalg.cho_solve((lower, True), jnp.concatenate([right_mat, unit], axis=1))
    vec_sol = jax.scipy.linalg.cho_solve((lower, True), right_vec)
    links = right_mat.shape[1]
    cols_sol = solved[:, :links]
    unit_sol = solved[:, links:]
    new_carry = (ramp_weight[:, None] * unit_sol[:count] * ramp_weight[None, :], ramp_weight * vec_sol[:count], ramp_weight[:, None] * cols_sol[:count])
    return ((unit_sol, vec_sol, cols_sol), new_carry)

def substitute(stored, carry, ramp_weight):
    unit_sol, vec_sol, cols_sol = stored
    vec_in, cols_in = carry
    count = ramp_weight.shape[0]
    step_vec = vec_sol + jnp.dot(unit_sol, vec_in, precision=highest)
    step_cols = cols_sol + jnp.dot(unit_sol, cols_in, precision=highest)
    return ((step_vec, step_cols), (ramp_weight * step_vec[:count], ramp_weight[:, None] * step_cols[:count]))

def scenario_solve(line_blocks, block_ids, weights, barrier_rows, grad_rows, link_mats, ramp_weight):
    periods = block_ids.shape[0]
    count = ramp_weight.shape[0]
    links = link_mats.shape[2]

    def forward(carry, inputs):
        period, id_row, weight_row, barrier_row, grad_row, link_mat = inputs
        selected = jnp.take(line_blocks, id_row, axis=0)
        end_factor = jnp.where((period == 0) | (period == periods - 1), 1.0, 2.0).astype(jnp.float32)
        hessian = period_hessian(selected, weight_row, barrier_row, ramp_weight, end_factor)
        stored, new_carry = eliminate(hessian, grad_row, link_mat, carry, ramp_weight)
        return (new_carry, stored)
    start = (jnp.zeros((count, count), jnp.float32), jnp.zeros((count,), jnp.float32), jnp.zeros((count, links), jnp.float32))
    _, stored = lax.scan(forward, start, (jnp.arange(periods, dtype=jnp.int32), block_ids, weights, barrier_rows, grad_rows, link_mats))

    def backward(carry, member):
        result, new_carry = substitute(member, carry, ramp_weight)
        return (new_carry, result)
    back_start = (jnp.zeros((count,), jnp.float32), jnp.zeros((count, links), jnp.float32))
    _, (step_vec, step_cols) = lax.scan(backward, back_start, stored, reverse=True)
    return (step_vec, step_cols)

def reference(line_blocks, binding, line_weight, barrier, gradient, link_columns, ramp_weight, link_diag, link_rhs):

    def one_scenario(inputs):
        block_ids, weights, barrier_rows, grad_rows, link_mats = inputs
        return scenario_solve(line_blocks, block_ids, weights, barrier_rows, grad_rows, link_mats, ramp_weight)
    step_vec, step_cols = lax.map(one_scenario, (binding, line_weight, barrier, gradient, link_columns))
    link_float = link_columns.astype(jnp.float32)
    inverse_count = 1.0 / (SCEN * PER)
    mat_total = jnp.einsum('spkl,spkm->lm', link_float, step_cols, precision=highest)
    vec_total = jnp.einsum('spkl,spk->l', link_float, step_vec, precision=highest)
    system = jnp.diag(link_diag) + inverse_count * mat_total
    right_side = inverse_count * vec_total - link_rhs
    lower = jnp.linalg.cholesky(system)
    link_step = jax.scipy.linalg.cho_solve((lower, True), right_side)
    newton_step = step_vec - jnp.einsum('spkl,l->spk', step_cols, link_step, precision=highest)
    return (newton_step, link_step)
```

```python
import jax
import jax.numpy as jnp
from jax import lax
from jax.sharding import PartitionSpec as P

highest = lax.Precision.HIGHEST


def period_hessian(selected, weights, barrier_row, ramp_weight, end_factor):
    order = selected.shape[-1]
    scaled = (weights[:, :, None] * selected.astype(jnp.float32)).astype(jnp.bfloat16)
    flat = selected.reshape(-1, order)
    scaled_flat = scaled.reshape(-1, order)
    hessian = lax.dot_general(
        flat, scaled_flat, (((0,), (0,)), ((), ())), preferred_element_type=jnp.float32
    )
    count = ramp_weight.shape[0]
    extra = jnp.concatenate([end_factor * ramp_weight, jnp.zeros((order - count,), jnp.float32)])
    return hessian + jnp.diag(barrier_row + extra)


def butterfly_sum(value, axes):
    for axis in axes:
        size = lax.axis_size(axis)
        step = 1
        while step < size:
            pairs = [(i, i ^ step) for i in range(size)]
            value = value + lax.ppermute(value, axis, pairs)
            step *= 2
    return value


def trsm(a, b, transpose=False):
    return lax.linalg.triangular_solve(a, b, left_side=True, lower=True, transpose_a=transpose)


def on_device(
    line_blocks,
    binding,
    line_weight,
    barrier,
    gradient,
    link_columns,
    ramp_weight,
    link_diag,
    link_rhs,
):
    block_ids = binding[0, 0]
    order = line_blocks.shape[2]
    count = ramp_weight.shape[0]
    links = link_columns.shape[-1]
    every_block = lax.all_gather(line_blocks, "line", axis=0, tiled=True)
    selected = jnp.take(every_block, block_ids, axis=0)
    shard = lax.axis_index("tm")
    shards = lax.axis_size("tm")
    end_factor = jnp.where((shard == 0) | (shard == shards - 1), 1.0, 2.0).astype(jnp.float32)
    hessian = period_hessian(selected, line_weight[0, 0], barrier[0, 0], ramp_weight, end_factor)

    link_float = link_columns[0, 0].astype(jnp.float32)
    rhs = jnp.concatenate([gradient[0, 0][:, None], link_float], axis=1)

    h_nn = hessian[count:, count:]
    h_nr = hessian[count:, :count]
    h_rr = hessian[:count, :count]
    l_nn = lax.linalg.cholesky(h_nn)
    solved = trsm(l_nn, jnp.concatenate([h_nr, rhs[count:]], axis=1))
    x_nr = solved[:, :count]
    y_n = solved[:, count:]
    schur = h_rr - jnp.dot(x_nr.T, x_nr, precision=highest)
    reduced = rhs[:count] - jnp.dot(x_nr.T, y_n, precision=highest)

    mine = jnp.concatenate([schur, reduced], axis=1)
    other = lax.ppermute(mine, "tm", [(0, 1), (1, 0)])
    first = shard == 0
    part0 = jnp.where(first, mine, other)
    part1 = jnp.where(first, other, mine)
    coupling = -jnp.diag(ramp_weight)
    system = jnp.concatenate(
        [
            jnp.concatenate([part0[:, :count], coupling], axis=1),
            jnp.concatenate([coupling, part1[:, :count]], axis=1),
        ],
        axis=0,
    )
    lower = lax.linalg.cholesky(system)
    ramp_both = jax.scipy.linalg.cho_solve(
        (lower, True), jnp.concatenate([part0[:, count:], part1[:, count:]], axis=0)
    )
    x_r = jnp.where(first, ramp_both[:count], ramp_both[count:])
    x_n = trsm(l_nn, y_n - jnp.dot(x_nr, x_r, precision=highest), transpose=True)
    solution_cols = jnp.concatenate([x_r, x_n], axis=0)
    step_vec = solution_cols[:, 0]
    step_cols = solution_cols[:, 1:]

    local = jnp.dot(link_float.T, solution_cols, precision=highest)
    total = butterfly_sum(local, ("tm", "scen", "line"))
    vec_total = total[:, 0]
    mat_total = total[:, 1:]
    inverse_count = 1.0 / (shards * lax.axis_size("scen") * lax.axis_size("line"))
    link_system = jnp.diag(link_diag) + inverse_count * mat_total
    right_side = inverse_count * vec_total - link_rhs
    link_lower = jnp.linalg.cholesky(link_system)
    link_step = jax.scipy.linalg.cho_solve((link_lower, True), right_side)
    newton_step = step_vec - jnp.dot(step_cols, link_step, precision=highest)
    return (newton_step[None, None], link_step)


def solution(mesh):
    return jax.shard_map(
        on_device,
        mesh=mesh,
        in_specs=(
            P("line", None, None),
            P(("scen", "line"), "tm", None),
            P(("scen", "line"), "tm", None, None),
            P(("scen", "line"), "tm", None),
            P(("scen", "line"), "tm", None),
            P(("scen", "line"), "tm", None, None),
            P(),
            P(),
            P(),
        ),
        out_specs=(P(("scen", "line"), "tm", None), P()),
        check_vma=False,
    )
```

```python
import jax
import jax.numpy as jnp
from jax import lax
from jax.sharding import PartitionSpec as P

highest = lax.Precision.HIGHEST


def period_hessian(selected, weights, barrier_row, ramp_weight, end_factor):
    order = selected.shape[-1]
    scaled = (weights[:, :, None] * selected.astype(jnp.float32)).astype(jnp.bfloat16)
    flat = selected.reshape(-1, order)
    scaled_flat = scaled.reshape(-1, order)
    hessian = lax.dot_general(
        flat, scaled_flat, (((0,), (0,)), ((), ())), preferred_element_type=jnp.float32
    )
    count = ramp_weight.shape[0]
    extra = jnp.concatenate([end_factor * ramp_weight, jnp.zeros((order - count,), jnp.float32)])
    return hessian + jnp.diag(barrier_row + extra)


def butterfly_sum(value, axes):
    for axis in axes:
        size = lax.axis_size(axis)
        step = 1
        while step < size:
            pairs = [(i, i ^ step) for i in range(size)]
            value = value + lax.ppermute(value, axis, pairs)
            step *= 2
    return value


def trsm(a, b, transpose=False):
    return lax.linalg.triangular_solve(a, b, left_side=True, lower=True, transpose_a=transpose)


def on_device(
    line_blocks,
    binding,
    line_weight,
    barrier,
    gradient,
    link_columns,
    ramp_weight,
    link_diag,
    link_rhs,
):
    block_ids = binding[0, 0]
    order = line_blocks.shape[2]
    count = ramp_weight.shape[0]
    links = link_columns.shape[-1]
    shard = lax.axis_index("tm")
    shards = lax.axis_size("tm")
    held = line_blocks.shape[0]
    pairs = line_blocks.reshape((held // 2, 2) + line_blocks.shape[1:])
    mine_half = lax.dynamic_index_in_dim(pairs, shard, axis=1, keepdims=False)
    half = lax.all_gather(mine_half, "line", axis=0, tiled=True)
    swap = [(0, 1), (1, 0)]
    partner_ids = lax.ppermute(block_ids, "tm", swap)
    for_partner = jnp.take(half, partner_ids // 2, axis=0)
    from_partner = lax.ppermute(for_partner, "tm", swap)
    own = jnp.take(half, block_ids // 2, axis=0)
    selected = jnp.where((block_ids % 2 == shard)[:, None, None], own, from_partner)
    end_factor = jnp.where((shard == 0) | (shard == shards - 1), 1.0, 2.0).astype(jnp.float32)
    hessian = period_hessian(selected, line_weight[0, 0], barrier[0, 0], ramp_weight, end_factor)

    link_float = link_columns[0, 0].astype(jnp.float32)
    rhs = jnp.concatenate([gradient[0, 0][:, None], link_float], axis=1)

    h_nn = hessian[count:, count:]
    h_nr = hessian[count:, :count]
    h_rr = hessian[:count, :count]
    l_nn = lax.linalg.cholesky(h_nn)
    solved = trsm(l_nn, jnp.concatenate([h_nr, rhs[count:]], axis=1))
    x_nr = solved[:, :count]
    y_n = solved[:, count:]
    schur = h_rr - jnp.dot(x_nr.T, x_nr, precision=highest)
    reduced = rhs[:count] - jnp.dot(x_nr.T, y_n, precision=highest)

    mine = jnp.concatenate([schur, reduced], axis=1)
    other = lax.ppermute(mine, "tm", [(0, 1), (1, 0)])
    first = shard == 0
    part0 = jnp.where(first, mine, other)
    part1 = jnp.where(first, other, mine)
    coupling = -jnp.diag(ramp_weight)
    system = jnp.concatenate(
        [
            jnp.concatenate([part0[:, :count], coupling], axis=1),
            jnp.concatenate([coupling, part1[:, :count]], axis=1),
        ],
        axis=0,
    )
    lower = lax.linalg.cholesky(system)
    ramp_both = jax.scipy.linalg.cho_solve(
        (lower, True), jnp.concatenate([part0[:, count:], part1[:, count:]], axis=0)
    )
    x_r = jnp.where(first, ramp_both[:count], ramp_both[count:])
    x_n = trsm(l_nn, y_n - jnp.dot(x_nr, x_r, precision=highest), transpose=True)
    solution_cols = jnp.concatenate([x_r, x_n], axis=0)
    step_vec = solution_cols[:, 0]
    step_cols = solution_cols[:, 1:]

    local = jnp.dot(link_float.T, solution_cols, precision=highest)
    total = butterfly_sum(local, ("tm", "scen", "line"))
    vec_total = total[:, 0]
    mat_total = total[:, 1:]
    inverse_count = 1.0 / (shards * lax.axis_size("scen") * lax.axis_size("line"))
    link_system = jnp.diag(link_diag) + inverse_count * mat_total
    right_side = inverse_count * vec_total - link_rhs
    link_lower = jnp.linalg.cholesky(link_system)
    link_step = jax.scipy.linalg.cho_solve((link_lower, True), right_side)
    newton_step = step_vec - jnp.dot(step_cols, link_step, precision=highest)
    return (newton_step[None, None], link_step)


def solution(mesh):
    return jax.shard_map(
        on_device,
        mesh=mesh,
        in_specs=(
            P("line", None, None),
            P(("scen", "line"), "tm", None),
            P(("scen", "line"), "tm", None, None),
            P(("scen", "line"), "tm", None),
            P(("scen", "line"), "tm", None),
            P(("scen", "line"), "tm", None, None),
            P(),
            P(),
            P(),
        ),
        out_specs=(P(("scen", "line"), "tm", None), P()),
        check_vma=False,
    )
```

```python
import jax
import jax.numpy as jnp
from jax import lax
from jax.sharding import PartitionSpec as P

highest = lax.Precision.HIGHEST


def period_hessian(selected, weights, barrier_row, ramp_weight, end_factor):
    order = selected.shape[-1]
    scaled = (weights[:, :, None] * selected.astype(jnp.float32)).astype(jnp.bfloat16)
    flat = selected.reshape(-1, order)
    scaled_flat = scaled.reshape(-1, order)
    hessian = lax.dot_general(
        flat, scaled_flat, (((0,), (0,)), ((), ())), preferred_element_type=jnp.float32
    )
    count = ramp_weight.shape[0]
    extra = jnp.concatenate([end_factor * ramp_weight, jnp.zeros((order - count,), jnp.float32)])
    return hessian + jnp.diag(barrier_row + extra)


def butterfly_sum(value, axes):
    for axis in axes:
        size = lax.axis_size(axis)
        step = 1
        while step < size:
            pairs = [(i, i ^ step) for i in range(size)]
            value = value + lax.ppermute(value, axis, pairs)
            step *= 2
    return value


BLOCK = 128


def diagonal_inverses(lower):
    blocks = lower.shape[0] // BLOCK
    diag = jnp.stack([lower[i * BLOCK:(i + 1) * BLOCK, i * BLOCK:(i + 1) * BLOCK] for i in range(blocks)])
    eye = jnp.broadcast_to(jnp.eye(BLOCK, dtype=lower.dtype), diag.shape)
    return lax.linalg.triangular_solve(diag, eye, left_side=True, lower=True)


def forward_solve(lower, inverses, rhs):
    parts = []
    for i in range(inverses.shape[0]):
        rows = slice(i * BLOCK, (i + 1) * BLOCK)
        acc = rhs[rows]
        if i:
            acc = acc - jnp.dot(lower[rows, : i * BLOCK], jnp.concatenate(parts, axis=0), precision=highest)
        parts.append(jnp.dot(inverses[i], acc, precision=highest))
    return jnp.concatenate(parts, axis=0)


def backward_solve(lower, inverses, rhs):
    count = inverses.shape[0]
    parts = [None] * count
    for i in reversed(range(count)):
        rows = slice(i * BLOCK, (i + 1) * BLOCK)
        acc = rhs[rows]
        if i < count - 1:
            later = jnp.concatenate(parts[i + 1:], axis=0)
            acc = acc - jnp.dot(lower[(i + 1) * BLOCK:, rows].T, later, precision=highest)
        parts[i] = jnp.dot(inverses[i].T, acc, precision=highest)
    return jnp.concatenate(parts, axis=0)


def on_device(
    line_blocks,
    binding,
    line_weight,
    barrier,
    gradient,
    link_columns,
    ramp_weight,
    link_diag,
    link_rhs,
):
    block_ids = binding[0, 0]
    order = line_blocks.shape[2]
    count = ramp_weight.shape[0]
    links = link_columns.shape[-1]
    shard = lax.axis_index("tm")
    shards = lax.axis_size("tm")
    held = line_blocks.shape[0]
    pairs = line_blocks.reshape((held // 2, 2) + line_blocks.shape[1:])
    mine_half = lax.dynamic_index_in_dim(pairs, shard, axis=1, keepdims=False)
    half = lax.all_gather(mine_half, "line", axis=0, tiled=True)
    swap = [(0, 1), (1, 0)]
    partner_ids = lax.ppermute(block_ids, "tm", swap)
    for_partner = jnp.take(half, partner_ids // 2, axis=0)
    from_partner = lax.ppermute(for_partner, "tm", swap)
    own = jnp.take(half, block_ids // 2, axis=0)
    selected = jnp.where((block_ids % 2 == shard)[:, None, None], own, from_partner)
    end_factor = jnp.where((shard == 0) | (shard == shards - 1), 1.0, 2.0).astype(jnp.float32)
    hessian = period_hessian(selected, line_weight[0, 0], barrier[0, 0], ramp_weight, end_factor)

    link_float = link_columns[0, 0].astype(jnp.float32)
    rhs = jnp.concatenate([gradient[0, 0][:, None], link_float], axis=1)

    h_nn = hessian[count:, count:]
    h_nr = hessian[count:, :count]
    h_rr = hessian[:count, :count]
    l_nn = lax.linalg.cholesky(h_nn)
    inv_nn = diagonal_inverses(l_nn)
    solved = forward_solve(l_nn, inv_nn, jnp.concatenate([h_nr, rhs[count:]], axis=1))
    x_nr = solved[:, :count]
    y_n = solved[:, count:]
    schur = h_rr - jnp.dot(x_nr.T, x_nr, precision=highest)
    reduced = rhs[:count] - jnp.dot(x_nr.T, y_n, precision=highest)

    mine = jnp.concatenate([schur, reduced], axis=1)
    other = lax.ppermute(mine, "tm", [(0, 1), (1, 0)])
    first = shard == 0
    part0 = jnp.where(first, mine, other)
    part1 = jnp.where(first, other, mine)
    coupling = -jnp.diag(ramp_weight)
    system = jnp.concatenate(
        [
            jnp.concatenate([part0[:, :count], coupling], axis=1),
            jnp.concatenate([coupling, part1[:, :count]], axis=1),
        ],
        axis=0,
    )
    lower = lax.linalg.cholesky(system)
    inv_sys = diagonal_inverses(lower)
    ramp_both = backward_solve(
        lower,
        inv_sys,
        forward_solve(lower, inv_sys, jnp.concatenate([part0[:, count:], part1[:, count:]], axis=0)),
    )
    x_r = jnp.where(first, ramp_both[:count], ramp_both[count:])
    x_n = backward_solve(l_nn, inv_nn, y_n - jnp.dot(x_nr, x_r, precision=highest))
    solution_cols = jnp.concatenate([x_r, x_n], axis=0)
    step_vec = solution_cols[:, 0]
    step_cols = solution_cols[:, 1:]

    local = jnp.dot(link_float.T, solution_cols, precision=highest)
    total = butterfly_sum(local, ("tm", "scen", "line"))
    vec_total = total[:, 0]
    mat_total = total[:, 1:]
    inverse_count = 1.0 / (shards * lax.axis_size("scen") * lax.axis_size("line"))
    link_system = jnp.diag(link_diag) + inverse_count * mat_total
    right_side = inverse_count * vec_total - link_rhs
    link_lower = jnp.linalg.cholesky(link_system)
    link_step = jax.scipy.linalg.cho_solve((link_lower, True), right_side)
    newton_step = step_vec - jnp.dot(step_cols, link_step, precision=highest)
    return (newton_step[None, None], link_step)


def solution(mesh):
    return jax.shard_map(
        on_device,
        mesh=mesh,
        in_specs=(
            P("line", None, None),
            P(("scen", "line"), "tm", None),
            P(("scen", "line"), "tm", None, None),
            P(("scen", "line"), "tm", None),
            P(("scen", "line"), "tm", None),
            P(("scen", "line"), "tm", None, None),
            P(),
            P(),
            P(),
        ),
        out_specs=(P(("scen", "line"), "tm", None), P()),
        check_vma=False,
    )
```

```python
import jax
import jax.numpy as jnp
from jax import lax
from jax.sharding import PartitionSpec as P

highest = lax.Precision.HIGHEST


def period_hessian(selected, weights, barrier_row, ramp_weight, end_factor):
    order = selected.shape[-1]
    scaled = (weights[:, :, None] * selected.astype(jnp.float32)).astype(jnp.bfloat16)
    flat = selected.reshape(-1, order)
    scaled_flat = scaled.reshape(-1, order)
    hessian = lax.dot_general(
        flat, scaled_flat, (((0,), (0,)), ((), ())), preferred_element_type=jnp.float32
    )
    count = ramp_weight.shape[0]
    extra = jnp.concatenate([end_factor * ramp_weight, jnp.zeros((order - count,), jnp.float32)])
    return hessian + jnp.diag(barrier_row + extra)


def butterfly_sum(value, axes):
    for axis in axes:
        size = lax.axis_size(axis)
        step = 1
        while step < size:
            pairs = [(i, i ^ step) for i in range(size)]
            value = value + lax.ppermute(value, axis, pairs)
            step *= 2
    return value


BLOCK = 128


def diagonal_inverses(lower):
    blocks = lower.shape[0] // BLOCK
    diag = jnp.stack([lower[i * BLOCK:(i + 1) * BLOCK, i * BLOCK:(i + 1) * BLOCK] for i in range(blocks)])
    row = lax.broadcasted_iota(jnp.int32, (BLOCK, BLOCK), 0)
    col = lax.broadcasted_iota(jnp.int32, (BLOCK, BLOCK), 1)
    eye = (row == col).astype(lower.dtype)
    inverse = eye / jnp.sum(diag * eye, axis=-1, keepdims=True)
    size = 1
    while size < BLOCK:
        below = (row // (2 * size) == col // (2 * size)) & ((row // size) % 2 == 1) & ((col // size) % 2 == 0)
        off = jnp.where(below, diag, 0.0)
        inverse = inverse - jnp.matmul(
            jnp.matmul(inverse, off, precision=highest), inverse, precision=highest
        )
        size *= 2
    return inverse


def forward_solve(lower, inverses, rhs):
    parts = []
    for i in range(inverses.shape[0]):
        rows = slice(i * BLOCK, (i + 1) * BLOCK)
        acc = rhs[rows]
        if i:
            acc = acc - jnp.dot(lower[rows, : i * BLOCK], jnp.concatenate(parts, axis=0), precision=highest)
        parts.append(jnp.dot(inverses[i], acc, precision=highest))
    return jnp.concatenate(parts, axis=0)


def backward_solve(lower, inverses, rhs):
    count = inverses.shape[0]
    parts = [None] * count
    for i in reversed(range(count)):
        rows = slice(i * BLOCK, (i + 1) * BLOCK)
        acc = rhs[rows]
        if i < count - 1:
            later = jnp.concatenate(parts[i + 1:], axis=0)
            acc = acc - jnp.dot(lower[(i + 1) * BLOCK:, rows].T, later, precision=highest)
        parts[i] = jnp.dot(inverses[i].T, acc, precision=highest)
    return jnp.concatenate(parts, axis=0)


def on_device(
    line_blocks,
    binding,
    line_weight,
    barrier,
    gradient,
    link_columns,
    ramp_weight,
    link_diag,
    link_rhs,
):
    block_ids = binding[0, 0]
    order = line_blocks.shape[2]
    count = ramp_weight.shape[0]
    links = link_columns.shape[-1]
    shard = lax.axis_index("tm")
    shards = lax.axis_size("tm")
    held = line_blocks.shape[0]
    pairs = line_blocks.reshape((held // 2, 2) + line_blocks.shape[1:])
    mine_half = lax.dynamic_index_in_dim(pairs, shard, axis=1, keepdims=False)
    half = lax.all_gather(mine_half, "line", axis=0, tiled=True)
    swap = [(0, 1), (1, 0)]
    partner_ids = lax.ppermute(block_ids, "tm", swap)
    for_partner = jnp.take(half, partner_ids // 2, axis=0)
    from_partner = lax.ppermute(for_partner, "tm", swap)
    own = jnp.take(half, block_ids // 2, axis=0)
    selected = jnp.where((block_ids % 2 == shard)[:, None, None], own, from_partner)
    end_factor = jnp.where((shard == 0) | (shard == shards - 1), 1.0, 2.0).astype(jnp.float32)
    hessian = period_hessian(selected, line_weight[0, 0], barrier[0, 0], ramp_weight, end_factor)

    link_float = link_columns[0, 0].astype(jnp.float32)
    rhs = jnp.concatenate([gradient[0, 0][:, None], link_float], axis=1)

    h_nn = hessian[count:, count:]
    h_nr = hessian[count:, :count]
    h_rr = hessian[:count, :count]
    l_nn = lax.linalg.cholesky(h_nn)
    inv_nn = diagonal_inverses(l_nn)
    solved = forward_solve(l_nn, inv_nn, jnp.concatenate([h_nr, rhs[count:]], axis=1))
    x_nr = solved[:, :count]
    y_n = solved[:, count:]
    schur = h_rr - jnp.dot(x_nr.T, x_nr, precision=highest)
    reduced = rhs[:count] - jnp.dot(x_nr.T, y_n, precision=highest)

    mine = jnp.concatenate([schur, reduced], axis=1)
    other = lax.ppermute(mine, "tm", [(0, 1), (1, 0)])
    first = shard == 0
    part0 = jnp.where(first, mine, other)
    part1 = jnp.where(first, other, mine)
    coupling = -jnp.diag(ramp_weight)
    system = jnp.concatenate(
        [
            jnp.concatenate([part0[:, :count], coupling], axis=1),
            jnp.concatenate([coupling, part1[:, :count]], axis=1),
        ],
        axis=0,
    )
    lower = lax.linalg.cholesky(system)
    inv_sys = diagonal_inverses(lower)
    ramp_both = backward_solve(
        lower,
        inv_sys,
        forward_solve(lower, inv_sys, jnp.concatenate([part0[:, count:], part1[:, count:]], axis=0)),
    )
    x_r = jnp.where(first, ramp_both[:count], ramp_both[count:])
    x_n = backward_solve(l_nn, inv_nn, y_n - jnp.dot(x_nr, x_r, precision=highest))
    solution_cols = jnp.concatenate([x_r, x_n], axis=0)
    step_vec = solution_cols[:, 0]
    step_cols = solution_cols[:, 1:]

    local = jnp.dot(link_float.T, solution_cols, precision=highest)
    total = butterfly_sum(local, ("tm", "scen", "line"))
    vec_total = total[:, 0]
    mat_total = total[:, 1:]
    inverse_count = 1.0 / (shards * lax.axis_size("scen") * lax.axis_size("line"))
    link_system = jnp.diag(link_diag) + inverse_count * mat_total
    right_side = inverse_count * vec_total - link_rhs
    link_lower = jnp.linalg.cholesky(link_system)
    link_step = jax.scipy.linalg.cho_solve((link_lower, True), right_side)
    newton_step = step_vec - jnp.dot(step_cols, link_step, precision=highest)
    return (newton_step[None, None], link_step)


def solution(mesh):
    return jax.shard_map(
        on_device,
        mesh=mesh,
        in_specs=(
            P("line", None, None),
            P(("scen", "line"), "tm", None),
            P(("scen", "line"), "tm", None, None),
            P(("scen", "line"), "tm", None),
            P(("scen", "line"), "tm", None),
            P(("scen", "line"), "tm", None, None),
            P(),
            P(),
            P(),
        ),
        out_specs=(P(("scen", "line"), "tm", None), P()),
        check_vma=False,
    )
```

```python
import jax
import jax.numpy as jnp
from jax import lax
from jax.sharding import PartitionSpec as P

highest = lax.Precision.HIGHEST


def period_hessian(selected, weights, barrier_row, ramp_weight, end_factor):
    order = selected.shape[-1]
    scaled = (weights[:, :, None] * selected.astype(jnp.float32)).astype(jnp.bfloat16)
    flat = selected.reshape(-1, order)
    scaled_flat = scaled.reshape(-1, order)
    hessian = lax.dot_general(
        flat, scaled_flat, (((0,), (0,)), ((), ())), preferred_element_type=jnp.float32
    )
    count = ramp_weight.shape[0]
    extra = jnp.concatenate([end_factor * ramp_weight, jnp.zeros((order - count,), jnp.float32)])
    return hessian + jnp.diag(barrier_row + extra)


def group_sum(value, axis, stride, size):
    if size == 1:
        return value
    length = lax.axis_size(axis)
    place = (lax.axis_index(axis) // stride) % size

    def member(i, k):
        return i - ((i // stride) % size) * stride + k * stride

    received = [value]
    for shift in range(1, size):
        pairs = [(i, member(i, ((i // stride) % size + shift) % size)) for i in range(length)]
        received.append(lax.ppermute(value, axis, pairs))
    ordered = jnp.take(jnp.stack(received), (place - jnp.arange(size)) % size, axis=0)
    total = ordered[0]
    for k in range(1, size):
        total = total + ordered[k]
    return total


def all_sum(value):
    value = group_sum(value, "tm", 1, lax.axis_size("tm"))
    value = group_sum(value, "scen", 1, lax.axis_size("scen"))
    line = lax.axis_size("line")
    inner = min(4, line)
    value = group_sum(value, "line", 1, inner)
    return group_sum(value, "line", inner, line // inner)


BLOCK = 128


def diagonal_inverses(lower):
    blocks = lower.shape[0] // BLOCK
    diag = jnp.stack([lower[i * BLOCK:(i + 1) * BLOCK, i * BLOCK:(i + 1) * BLOCK] for i in range(blocks)])
    row = lax.broadcasted_iota(jnp.int32, (BLOCK, BLOCK), 0)
    col = lax.broadcasted_iota(jnp.int32, (BLOCK, BLOCK), 1)
    eye = (row == col).astype(lower.dtype)
    inverse = eye / jnp.sum(diag * eye, axis=-1, keepdims=True)
    size = 1
    while size < BLOCK:
        below = (row // (2 * size) == col // (2 * size)) & ((row // size) % 2 == 1) & ((col // size) % 2 == 0)
        off = jnp.where(below, diag, 0.0)
        inverse = inverse - jnp.matmul(
            jnp.matmul(inverse, off, precision=highest), inverse, precision=highest
        )
        size *= 2
    return inverse


def forward_solve(lower, inverses, rhs):
    parts = []
    for i in range(inverses.shape[0]):
        rows = slice(i * BLOCK, (i + 1) * BLOCK)
        acc = rhs[rows]
        if i:
            acc = acc - jnp.dot(lower[rows, : i * BLOCK], jnp.concatenate(parts, axis=0), precision=highest)
        parts.append(jnp.dot(inverses[i], acc, precision=highest))
    return jnp.concatenate(parts, axis=0)


def backward_solve(lower, inverses, rhs):
    count = inverses.shape[0]
    parts = [None] * count
    for i in reversed(range(count)):
        rows = slice(i * BLOCK, (i + 1) * BLOCK)
        acc = rhs[rows]
        if i < count - 1:
            later = jnp.concatenate(parts[i + 1:], axis=0)
            acc = acc - jnp.dot(lower[(i + 1) * BLOCK:, rows].T, later, precision=highest)
        parts[i] = jnp.dot(inverses[i].T, acc, precision=highest)
    return jnp.concatenate(parts, axis=0)


def on_device(
    line_blocks,
    binding,
    line_weight,
    barrier,
    gradient,
    link_columns,
    ramp_weight,
    link_diag,
    link_rhs,
):
    block_ids = binding[0, 0]
    order = line_blocks.shape[2]
    count = ramp_weight.shape[0]
    links = link_columns.shape[-1]
    shard = lax.axis_index("tm")
    shards = lax.axis_size("tm")
    held = line_blocks.shape[0]
    pairs = line_blocks.reshape((held // 2, 2) + line_blocks.shape[1:])
    mine_half = lax.dynamic_index_in_dim(pairs, shard, axis=1, keepdims=False)
    half = lax.all_gather(mine_half, "line", axis=0, tiled=True)
    swap = [(0, 1), (1, 0)]
    partner_ids = lax.ppermute(block_ids, "tm", swap)
    for_partner = jnp.take(half, partner_ids // 2, axis=0)
    from_partner = lax.ppermute(for_partner, "tm", swap)
    own = jnp.take(half, block_ids // 2, axis=0)
    selected = jnp.where((block_ids % 2 == shard)[:, None, None], own, from_partner)
    end_factor = jnp.where((shard == 0) | (shard == shards - 1), 1.0, 2.0).astype(jnp.float32)
    hessian = period_hessian(selected, line_weight[0, 0], barrier[0, 0], ramp_weight, end_factor)

    link_float = link_columns[0, 0].astype(jnp.float32)
    rhs = jnp.concatenate([gradient[0, 0][:, None], link_float], axis=1)

    h_nn = hessian[count:, count:]
    h_nr = hessian[count:, :count]
    h_rr = hessian[:count, :count]
    l_nn = lax.linalg.cholesky(h_nn)
    inv_nn = diagonal_inverses(l_nn)
    solved = forward_solve(l_nn, inv_nn, jnp.concatenate([h_nr, rhs[count:]], axis=1))
    x_nr = solved[:, :count]
    y_n = solved[:, count:]
    schur = h_rr - jnp.dot(x_nr.T, x_nr, precision=highest)
    reduced = rhs[:count] - jnp.dot(x_nr.T, y_n, precision=highest)

    mine = jnp.concatenate([schur, reduced], axis=1)
    other = lax.ppermute(mine, "tm", [(0, 1), (1, 0)])
    first = shard == 0
    part0 = jnp.where(first, mine, other)
    part1 = jnp.where(first, other, mine)
    coupling = -jnp.diag(ramp_weight)
    system = jnp.concatenate(
        [
            jnp.concatenate([part0[:, :count], coupling], axis=1),
            jnp.concatenate([coupling, part1[:, :count]], axis=1),
        ],
        axis=0,
    )
    lower = lax.linalg.cholesky(system)
    inv_sys = diagonal_inverses(lower)
    ramp_both = backward_solve(
        lower,
        inv_sys,
        forward_solve(lower, inv_sys, jnp.concatenate([part0[:, count:], part1[:, count:]], axis=0)),
    )
    x_r = jnp.where(first, ramp_both[:count], ramp_both[count:])
    x_n = backward_solve(l_nn, inv_nn, y_n - jnp.dot(x_nr, x_r, precision=highest))
    solution_cols = jnp.concatenate([x_r, x_n], axis=0)
    step_vec = solution_cols[:, 0]
    step_cols = solution_cols[:, 1:]

    local = jnp.dot(link_float.T, solution_cols, precision=highest)
    total = all_sum(local)
    vec_total = total[:, 0]
    mat_total = total[:, 1:]
    inverse_count = 1.0 / (shards * lax.axis_size("scen") * lax.axis_size("line"))
    link_system = jnp.diag(link_diag) + inverse_count * mat_total
    right_side = inverse_count * vec_total - link_rhs
    link_lower = jnp.linalg.cholesky(link_system)
    link_step = jax.scipy.linalg.cho_solve((link_lower, True), right_side)
    newton_step = step_vec - jnp.dot(step_cols, link_step, precision=highest)
    return (newton_step[None, None], link_step)


def solution(mesh):
    return jax.shard_map(
        on_device,
        mesh=mesh,
        in_specs=(
            P("line", None, None),
            P(("scen", "line"), "tm", None),
            P(("scen", "line"), "tm", None, None),
            P(("scen", "line"), "tm", None),
            P(("scen", "line"), "tm", None),
            P(("scen", "line"), "tm", None, None),
            P(),
            P(),
            P(),
        ),
        out_specs=(P(("scen", "line"), "tm", None), P()),
        check_vma=False,
    )
```

```python
import jax
import jax.numpy as jnp
from jax import lax
from jax.sharding import PartitionSpec as P

highest = lax.Precision.HIGHEST


def period_hessian(selected, weights, barrier_row, ramp_weight, end_factor):
    order = selected.shape[-1]
    scaled = (weights[:, :, None] * selected.astype(jnp.float32)).astype(jnp.bfloat16)
    flat = selected.reshape(-1, order)
    scaled_flat = scaled.reshape(-1, order)
    hessian = lax.dot_general(
        flat, scaled_flat, (((0,), (0,)), ((), ())), preferred_element_type=jnp.float32
    )
    count = ramp_weight.shape[0]
    extra = jnp.concatenate([end_factor * ramp_weight, jnp.zeros((order - count,), jnp.float32)])
    return hessian + jnp.diag(barrier_row + extra)


def group_sum(value, axis, stride, size):
    if size == 1:
        return value
    length = lax.axis_size(axis)
    place = (lax.axis_index(axis) // stride) % size

    def member(i, k):
        return i - ((i // stride) % size) * stride + k * stride

    received = [value]
    for shift in range(1, size):
        pairs = [(i, member(i, ((i // stride) % size + shift) % size)) for i in range(length)]
        received.append(lax.ppermute(value, axis, pairs))
    ordered = jnp.take(jnp.stack(received), (place - jnp.arange(size)) % size, axis=0)
    total = ordered[0]
    for k in range(1, size):
        total = total + ordered[k]
    return total


def all_sum(value):
    value = group_sum(value, "tm", 1, lax.axis_size("tm"))
    value = group_sum(value, "scen", 1, lax.axis_size("scen"))
    line = lax.axis_size("line")
    inner = min(4, line)
    value = group_sum(value, "line", 1, inner)
    return group_sum(value, "line", inner, line // inner)


BLOCK = 128


def triangular_inverses(diag):
    size_of = diag.shape[-1]
    row = lax.broadcasted_iota(jnp.int32, (size_of, size_of), 0)
    col = lax.broadcasted_iota(jnp.int32, (size_of, size_of), 1)
    eye = (row == col).astype(diag.dtype)
    inverse = eye / jnp.sum(diag * eye, axis=-1, keepdims=True)
    size = 1
    while size < size_of:
        below = (row // (2 * size) == col // (2 * size)) & ((row // size) % 2 == 1) & ((col // size) % 2 == 0)
        off = jnp.where(below, diag, 0.0)
        inverse = inverse - jnp.matmul(
            jnp.matmul(inverse, off, precision=highest), inverse, precision=highest
        )
        size *= 2
    return inverse


def blocked_cholesky(matrix):
    order = matrix.shape[0]
    blocks = order // BLOCK
    trailing = matrix
    columns = []
    inverses = []
    for k in range(blocks):
        factor = lax.linalg.cholesky(trailing[:BLOCK, :BLOCK])
        inverse = triangular_inverses(factor)
        inverses.append(inverse)
        if k < blocks - 1:
            panel = jnp.dot(trailing[BLOCK:, :BLOCK], inverse.T, precision=highest)
            trailing = trailing[BLOCK:, BLOCK:] - jnp.dot(panel, panel.T, precision=highest)
            column = jnp.concatenate([factor, panel], axis=0)
        else:
            column = factor
        columns.append(jnp.pad(column, ((k * BLOCK, 0), (0, 0))))
    return jnp.concatenate(columns, axis=1), jnp.stack(inverses)


def forward_solve(lower, inverses, rhs):
    parts = []
    for i in range(inverses.shape[0]):
        rows = slice(i * BLOCK, (i + 1) * BLOCK)
        acc = rhs[rows]
        if i:
            acc = acc - jnp.dot(lower[rows, : i * BLOCK], jnp.concatenate(parts, axis=0), precision=highest)
        parts.append(jnp.dot(inverses[i], acc, precision=highest))
    return jnp.concatenate(parts, axis=0)


def backward_solve(lower, inverses, rhs):
    count = inverses.shape[0]
    parts = [None] * count
    for i in reversed(range(count)):
        rows = slice(i * BLOCK, (i + 1) * BLOCK)
        acc = rhs[rows]
        if i < count - 1:
            later = jnp.concatenate(parts[i + 1:], axis=0)
            acc = acc - jnp.dot(lower[(i + 1) * BLOCK:, rows].T, later, precision=highest)
        parts[i] = jnp.dot(inverses[i].T, acc, precision=highest)
    return jnp.concatenate(parts, axis=0)


def on_device(
    line_blocks,
    binding,
    line_weight,
    barrier,
    gradient,
    link_columns,
    ramp_weight,
    link_diag,
    link_rhs,
):
    block_ids = binding[0, 0]
    order = line_blocks.shape[2]
    count = ramp_weight.shape[0]
    links = link_columns.shape[-1]
    shard = lax.axis_index("tm")
    shards = lax.axis_size("tm")
    held = line_blocks.shape[0]
    pairs = line_blocks.reshape((held // 2, 2) + line_blocks.shape[1:])
    mine_half = lax.dynamic_index_in_dim(pairs, shard, axis=1, keepdims=False)
    half = lax.all_gather(mine_half, "line", axis=0, tiled=True)
    swap = [(0, 1), (1, 0)]
    partner_ids = lax.ppermute(block_ids, "tm", swap)
    for_partner = jnp.take(half, partner_ids // 2, axis=0)
    from_partner = lax.ppermute(for_partner, "tm", swap)
    own = jnp.take(half, block_ids // 2, axis=0)
    selected = jnp.where((block_ids % 2 == shard)[:, None, None], own, from_partner)
    end_factor = jnp.where((shard == 0) | (shard == shards - 1), 1.0, 2.0).astype(jnp.float32)
    hessian = period_hessian(selected, line_weight[0, 0], barrier[0, 0], ramp_weight, end_factor)
    hessian = (hessian + hessian.T) / 2

    link_float = link_columns[0, 0].astype(jnp.float32)
    rhs = jnp.concatenate([gradient[0, 0][:, None], link_float], axis=1)

    h_nn = hessian[count:, count:]
    h_nr = hessian[count:, :count]
    h_rr = hessian[:count, :count]
    l_nn, inv_nn = blocked_cholesky(h_nn)
    solved = forward_solve(l_nn, inv_nn, jnp.concatenate([h_nr, rhs[count:]], axis=1))
    x_nr = solved[:, :count]
    y_n = solved[:, count:]
    schur = h_rr - jnp.dot(x_nr.T, x_nr, precision=highest)
    reduced = rhs[:count] - jnp.dot(x_nr.T, y_n, precision=highest)

    mine = jnp.concatenate([schur, reduced], axis=1)
    other = lax.ppermute(mine, "tm", [(0, 1), (1, 0)])
    first = shard == 0
    part0 = jnp.where(first, mine, other)
    part1 = jnp.where(first, other, mine)
    coupling = -jnp.diag(ramp_weight)
    system = jnp.concatenate(
        [
            jnp.concatenate([part0[:, :count], coupling], axis=1),
            jnp.concatenate([coupling, part1[:, :count]], axis=1),
        ],
        axis=0,
    )
    lower, inv_sys = blocked_cholesky(system)
    ramp_both = backward_solve(
        lower,
        inv_sys,
        forward_solve(lower, inv_sys, jnp.concatenate([part0[:, count:], part1[:, count:]], axis=0)),
    )
    x_r = jnp.where(first, ramp_both[:count], ramp_both[count:])
    x_n = backward_solve(l_nn, inv_nn, y_n - jnp.dot(x_nr, x_r, precision=highest))
    solution_cols = jnp.concatenate([x_r, x_n], axis=0)
    step_vec = solution_cols[:, 0]
    step_cols = solution_cols[:, 1:]

    local = jnp.dot(link_float.T, solution_cols, precision=highest)
    total = all_sum(local)
    vec_total = total[:, 0]
    mat_total = total[:, 1:]
    inverse_count = 1.0 / (shards * lax.axis_size("scen") * lax.axis_size("line"))
    link_system = jnp.diag(link_diag) + inverse_count * mat_total
    right_side = inverse_count * vec_total - link_rhs
    link_lower, link_inv = blocked_cholesky(link_system)
    link_step = backward_solve(
        link_lower, link_inv, forward_solve(link_lower, link_inv, right_side[:, None])
    )[:, 0]
    newton_step = step_vec - jnp.dot(step_cols, link_step, precision=highest)
    return (newton_step[None, None], link_step)


def solution(mesh):
    return jax.shard_map(
        on_device,
        mesh=mesh,
        in_specs=(
            P("line", None, None),
            P(("scen", "line"), "tm", None),
            P(("scen", "line"), "tm", None, None),
            P(("scen", "line"), "tm", None),
            P(("scen", "line"), "tm", None),
            P(("scen", "line"), "tm", None, None),
            P(),
            P(),
            P(),
        ),
        out_specs=(P(("scen", "line"), "tm", None), P()),
        check_vma=False,
    )
```

```python
import jax
import jax.numpy as jnp
from jax import lax
from jax.sharding import PartitionSpec as P

highest = lax.Precision.HIGHEST


def period_hessian(selected, weights, barrier_row, ramp_weight, end_factor):
    order = selected.shape[-1]
    scaled = (weights[:, :, None] * selected.astype(jnp.float32)).astype(jnp.bfloat16)
    flat = selected.reshape(-1, order)
    scaled_flat = scaled.reshape(-1, order)
    hessian = lax.dot_general(
        flat, scaled_flat, (((0,), (0,)), ((), ())), preferred_element_type=jnp.float32
    )
    transposed = lax.dot_general(
        scaled_flat, flat, (((0,), (0,)), ((), ())), preferred_element_type=jnp.float32
    )
    count = ramp_weight.shape[0]
    extra = jnp.concatenate([end_factor * ramp_weight, jnp.zeros((order - count,), jnp.float32)])
    return (hessian + transposed) / 2 + jnp.diag(barrier_row + extra)


def group_sum(value, axis, stride, size):
    if size == 1:
        return value
    length = lax.axis_size(axis)
    place = (lax.axis_index(axis) // stride) % size

    def member(i, k):
        return i - ((i // stride) % size) * stride + k * stride

    received = [value]
    for shift in range(1, size):
        pairs = [(i, member(i, ((i // stride) % size + shift) % size)) for i in range(length)]
        received.append(lax.ppermute(value, axis, pairs))
    ordered = jnp.take(jnp.stack(received), (place - jnp.arange(size)) % size, axis=0)
    total = ordered[0]
    for k in range(1, size):
        total = total + ordered[k]
    return total


def all_sum(value):
    value = group_sum(value, "tm", 1, lax.axis_size("tm"))
    value = group_sum(value, "scen", 1, lax.axis_size("scen"))
    line = lax.axis_size("line")
    inner = min(4, line)
    value = group_sum(value, "line", 1, inner)
    outer = line // inner
    first = 2 if outer % 2 == 0 else 1
    value = group_sum(value, "line", inner, first)
    return group_sum(value, "line", inner * first, outer // first)


BLOCK = 128


def triangular_inverses(diag):
    size_of = diag.shape[-1]
    row = lax.broadcasted_iota(jnp.int32, (size_of, size_of), 0)
    col = lax.broadcasted_iota(jnp.int32, (size_of, size_of), 1)
    eye = (row == col).astype(diag.dtype)
    inverse = eye / jnp.sum(diag * eye, axis=-1, keepdims=True)
    size = 1
    while size < size_of:
        below = (row // (2 * size) == col // (2 * size)) & ((row // size) % 2 == 1) & ((col // size) % 2 == 0)
        off = jnp.where(below, diag, 0.0)
        inverse = inverse - jnp.matmul(
            jnp.matmul(inverse, off, precision=highest), inverse, precision=highest
        )
        size *= 2
    return inverse


def blocked_cholesky(matrix):
    order = matrix.shape[0]
    blocks = order // BLOCK
    trailing = matrix
    columns = []
    inverses = []
    for k in range(blocks):
        factor = lax.linalg.cholesky(trailing[:BLOCK, :BLOCK])
        inverse = triangular_inverses(factor)
        inverses.append(inverse)
        if k < blocks - 1:
            panel = jnp.dot(trailing[BLOCK:, :BLOCK], inverse.T, precision=highest)
            trailing = trailing[BLOCK:, BLOCK:] - jnp.dot(panel, panel.T, precision=highest)
            column = jnp.concatenate([factor, panel], axis=0)
        else:
            column = factor
        columns.append(jnp.pad(column, ((k * BLOCK, 0), (0, 0))))
    return jnp.concatenate(columns, axis=1), jnp.stack(inverses)


def forward_solve(lower, inverses, rhs):
    parts = []
    for i in range(inverses.shape[0]):
        rows = slice(i * BLOCK, (i + 1) * BLOCK)
        acc = rhs[rows]
        if i:
            acc = acc - jnp.dot(lower[rows, : i * BLOCK], jnp.concatenate(parts, axis=0), precision=highest)
        parts.append(jnp.dot(inverses[i], acc, precision=highest))
    return jnp.concatenate(parts, axis=0)


def backward_solve(lower, inverses, rhs):
    count = inverses.shape[0]
    parts = [None] * count
    for i in reversed(range(count)):
        rows = slice(i * BLOCK, (i + 1) * BLOCK)
        acc = rhs[rows]
        if i < count - 1:
            later = jnp.concatenate(parts[i + 1:], axis=0)
            acc = acc - jnp.dot(lower[(i + 1) * BLOCK:, rows].T, later, precision=highest)
        parts[i] = jnp.dot(inverses[i].T, acc, precision=highest)
    return jnp.concatenate(parts, axis=0)


def on_device(
    line_blocks,
    binding,
    line_weight,
    barrier,
    gradient,
    link_columns,
    ramp_weight,
    link_diag,
    link_rhs,
):
    block_ids = binding[0, 0]
    order = line_blocks.shape[2]
    count = ramp_weight.shape[0]
    links = link_columns.shape[-1]
    shard = lax.axis_index("tm")
    shards = lax.axis_size("tm")
    held = line_blocks.shape[0]
    pairs = line_blocks.reshape((held // 2, 2) + line_blocks.shape[1:])
    mine_half = lax.dynamic_index_in_dim(pairs, shard, axis=1, keepdims=False)
    half = lax.all_gather(mine_half, "line", axis=0, tiled=True)
    swap = [(0, 1), (1, 0)]
    partner_ids = lax.ppermute(block_ids, "tm", swap)
    for_partner = jnp.take(half, partner_ids // 2, axis=0)
    from_partner = lax.ppermute(for_partner, "tm", swap)
    own = jnp.take(half, block_ids // 2, axis=0)
    selected = jnp.where((block_ids % 2 == shard)[:, None, None], own, from_partner)
    end_factor = jnp.where((shard == 0) | (shard == shards - 1), 1.0, 2.0).astype(jnp.float32)
    hessian = period_hessian(selected, line_weight[0, 0], barrier[0, 0], ramp_weight, end_factor)

    link_float = link_columns[0, 0].astype(jnp.float32)
    rhs = jnp.concatenate([gradient[0, 0][:, None], link_float], axis=1)

    h_nn = hessian[count:, count:]
    h_nr = hessian[count:, :count]
    h_rr = hessian[:count, :count]
    l_nn, inv_nn = blocked_cholesky(h_nn)
    solved = forward_solve(l_nn, inv_nn, jnp.concatenate([h_nr, rhs[count:]], axis=1))
    x_nr = solved[:, :count]
    y_n = solved[:, count:]
    schur = h_rr - jnp.dot(x_nr.T, x_nr, precision=highest)
    reduced = rhs[:count] - jnp.dot(x_nr.T, y_n, precision=highest)

    mine = jnp.concatenate([schur, reduced], axis=1)
    other = lax.ppermute(mine, "tm", [(0, 1), (1, 0)])
    first = shard == 0
    part0 = jnp.where(first, mine, other)
    part1 = jnp.where(first, other, mine)
    coupling = -jnp.diag(ramp_weight)
    system = jnp.concatenate(
        [
            jnp.concatenate([part0[:, :count], coupling], axis=1),
            jnp.concatenate([coupling, part1[:, :count]], axis=1),
        ],
        axis=0,
    )
    lower, inv_sys = blocked_cholesky(system)
    ramp_both = backward_solve(
        lower,
        inv_sys,
        forward_solve(lower, inv_sys, jnp.concatenate([part0[:, count:], part1[:, count:]], axis=0)),
    )
    x_r = jnp.where(first, ramp_both[:count], ramp_both[count:])
    x_n = backward_solve(l_nn, inv_nn, y_n - jnp.dot(x_nr, x_r, precision=highest))
    solution_cols = jnp.concatenate([x_r, x_n], axis=0)
    step_vec = solution_cols[:, 0]
    step_cols = solution_cols[:, 1:]

    local = jnp.dot(link_float.T, solution_cols, precision=highest)
    total = all_sum(local)
    vec_total = total[:, 0]
    mat_total = total[:, 1:]
    inverse_count = 1.0 / (shards * lax.axis_size("scen") * lax.axis_size("line"))
    link_system = jnp.diag(link_diag) + inverse_count * mat_total
    right_side = inverse_count * vec_total - link_rhs
    link_lower, link_inv = blocked_cholesky(link_system)
    link_step = backward_solve(
        link_lower, link_inv, forward_solve(link_lower, link_inv, right_side[:, None])
    )[:, 0]
    newton_step = step_vec - jnp.dot(step_cols, link_step, precision=highest)
    return (newton_step[None, None], link_step)


def solution(mesh):
    return jax.shard_map(
        on_device,
        mesh=mesh,
        in_specs=(
            P("line", None, None),
            P(("scen", "line"), "tm", None),
            P(("scen", "line"), "tm", None, None),
            P(("scen", "line"), "tm", None),
            P(("scen", "line"), "tm", None),
            P(("scen", "line"), "tm", None, None),
            P(),
            P(),
            P(),
        ),
        out_specs=(P(("scen", "line"), "tm", None), P()),
        check_vma=False,
    )
```

```python
import jax
import jax.numpy as jnp
from jax import lax
from jax.sharding import PartitionSpec as P

highest = lax.Precision.HIGHEST


def period_hessian(selected, weights, barrier_row, ramp_weight, end_factor):
    order = selected.shape[-1]
    scaled = (weights[:, :, None] * selected.astype(jnp.float32)).astype(jnp.bfloat16)
    flat = selected.reshape(-1, order)
    scaled_flat = scaled.reshape(-1, order)
    hessian = lax.dot_general(
        flat, scaled_flat, (((0,), (0,)), ((), ())), preferred_element_type=jnp.float32
    )
    transposed = lax.dot_general(
        scaled_flat, flat, (((0,), (0,)), ((), ())), preferred_element_type=jnp.float32
    )
    count = ramp_weight.shape[0]
    extra = jnp.concatenate([end_factor * ramp_weight, jnp.zeros((order - count,), jnp.float32)])
    return (hessian + transposed) / 2 + jnp.diag(barrier_row + extra)


def group_sum(value, axis, stride, size):
    if size == 1:
        return value
    length = lax.axis_size(axis)
    place = (lax.axis_index(axis) // stride) % size

    def member(i, k):
        return i - ((i // stride) % size) * stride + k * stride

    received = [value]
    for shift in range(1, size):
        pairs = [(i, member(i, ((i // stride) % size + shift) % size)) for i in range(length)]
        received.append(lax.ppermute(value, axis, pairs))
    ordered = jnp.take(jnp.stack(received), (place - jnp.arange(size)) % size, axis=0)
    total = ordered[0]
    for k in range(1, size):
        total = total + ordered[k]
    return total


def all_sum(value):
    value = group_sum(value, "tm", 1, lax.axis_size("tm"))
    value = group_sum(value, "scen", 1, lax.axis_size("scen"))
    line = lax.axis_size("line")
    inner = min(4, line)
    value = group_sum(value, "line", 1, inner)
    return group_sum(value, "line", inner, line // inner)


BLOCK = 128


def triangular_inverses(diag):
    size_of = diag.shape[-1]
    row = lax.broadcasted_iota(jnp.int32, (size_of, size_of), 0)
    col = lax.broadcasted_iota(jnp.int32, (size_of, size_of), 1)
    eye = (row == col).astype(diag.dtype)
    inverse = eye / jnp.sum(diag * eye, axis=-1, keepdims=True)
    size = 1
    while size < size_of:
        below = (row // (2 * size) == col // (2 * size)) & ((row // size) % 2 == 1) & ((col // size) % 2 == 0)
        off = jnp.where(below, diag, 0.0)
        inverse = inverse - jnp.matmul(
            jnp.matmul(inverse, off, precision=highest), inverse, precision=highest
        )
        size *= 2
    return inverse


def blocked_cholesky(matrix):
    order = matrix.shape[0]
    blocks = order // BLOCK
    trailing = matrix
    columns = []
    inverses = []
    for k in range(blocks):
        factor = lax.linalg.cholesky(trailing[:BLOCK, :BLOCK])
        inverse = triangular_inverses(factor)
        inverses.append(inverse)
        if k < blocks - 1:
            panel = jnp.dot(trailing[BLOCK:, :BLOCK], inverse.T, precision=highest)
            trailing = trailing[BLOCK:, BLOCK:] - jnp.dot(panel, panel.T, precision=highest)
            column = jnp.concatenate([factor, panel], axis=0)
        else:
            column = factor
        columns.append(jnp.pad(column, ((k * BLOCK, 0), (0, 0))))
    return jnp.concatenate(columns, axis=1), jnp.stack(inverses)


def forward_solve(lower, inverses, rhs):
    parts = []
    for i in range(inverses.shape[0]):
        rows = slice(i * BLOCK, (i + 1) * BLOCK)
        acc = rhs[rows]
        if i:
            acc = acc - jnp.dot(lower[rows, : i * BLOCK], jnp.concatenate(parts, axis=0), precision=highest)
        parts.append(jnp.dot(inverses[i], acc, precision=highest))
    return jnp.concatenate(parts, axis=0)


def backward_solve(lower, inverses, rhs):
    count = inverses.shape[0]
    parts = [None] * count
    for i in reversed(range(count)):
        rows = slice(i * BLOCK, (i + 1) * BLOCK)
        acc = rhs[rows]
        if i < count - 1:
            later = jnp.concatenate(parts[i + 1:], axis=0)
            acc = acc - jnp.dot(lower[(i + 1) * BLOCK:, rows].T, later, precision=highest)
        parts[i] = jnp.dot(inverses[i].T, acc, precision=highest)
    return jnp.concatenate(parts, axis=0)


def on_device(
    line_blocks,
    binding,
    line_weight,
    barrier,
    gradient,
    link_columns,
    ramp_weight,
    link_diag,
    link_rhs,
):
    block_ids = binding[0, 0]
    order = line_blocks.shape[2]
    count = ramp_weight.shape[0]
    links = link_columns.shape[-1]
    shard = lax.axis_index("tm")
    shards = lax.axis_size("tm")
    held = line_blocks.shape[0]
    pairs = line_blocks.reshape((held // 2, 2) + line_blocks.shape[1:])
    mine_half = lax.dynamic_index_in_dim(pairs, shard, axis=1, keepdims=False)
    half = lax.all_gather(mine_half, "line", axis=0, tiled=True)
    swap = [(0, 1), (1, 0)]
    partner_ids = lax.ppermute(block_ids, "tm", swap)
    for_partner = jnp.take(half, partner_ids // 2, axis=0)
    from_partner = lax.ppermute(for_partner, "tm", swap)
    own = jnp.take(half, block_ids // 2, axis=0)
    selected = jnp.where((block_ids % 2 == shard)[:, None, None], own, from_partner)
    end_factor = jnp.where((shard == 0) | (shard == shards - 1), 1.0, 2.0).astype(jnp.float32)
    hessian = period_hessian(selected, line_weight[0, 0], barrier[0, 0], ramp_weight, end_factor)

    link_float = link_columns[0, 0].astype(jnp.float32)
    rhs = jnp.concatenate([gradient[0, 0][:, None], link_float], axis=1)

    h_nn = hessian[count:, count:]
    h_nr = hessian[count:, :count]
    h_rr = hessian[:count, :count]
    l_nn, inv_nn = blocked_cholesky(h_nn)
    solved = forward_solve(l_nn, inv_nn, jnp.concatenate([h_nr, rhs[count:]], axis=1))
    x_nr = solved[:, :count]
    y_n = solved[:, count:]
    schur = h_rr - jnp.dot(x_nr.T, x_nr, precision=highest)
    reduced = rhs[:count] - jnp.dot(x_nr.T, y_n, precision=highest)

    mine = jnp.concatenate([schur, reduced], axis=1)
    other = lax.ppermute(mine, "tm", [(0, 1), (1, 0)])
    first = shard == 0
    part0 = jnp.where(first, mine, other)
    part1 = jnp.where(first, other, mine)
    coupling = -jnp.diag(ramp_weight)
    system = jnp.concatenate(
        [
            jnp.concatenate([part0[:, :count], coupling], axis=1),
            jnp.concatenate([coupling, part1[:, :count]], axis=1),
        ],
        axis=0,
    )
    lower, inv_sys = blocked_cholesky(system)
    ramp_both = backward_solve(
        lower,
        inv_sys,
        forward_solve(lower, inv_sys, jnp.concatenate([part0[:, count:], part1[:, count:]], axis=0)),
    )
    x_r = jnp.where(first, ramp_both[:count], ramp_both[count:])
    x_n = backward_solve(l_nn, inv_nn, y_n - jnp.dot(x_nr, x_r, precision=highest))
    solution_cols = jnp.concatenate([x_r, x_n], axis=0)
    step_vec = solution_cols[:, 0]
    step_cols = solution_cols[:, 1:]

    local = jnp.dot(link_float.T, solution_cols, precision=highest)
    total = all_sum(local)
    vec_total = total[:, 0]
    mat_total = total[:, 1:]
    inverse_count = 1.0 / (shards * lax.axis_size("scen") * lax.axis_size("line"))
    link_system = jnp.diag(link_diag) + inverse_count * mat_total
    right_side = inverse_count * vec_total - link_rhs
    link_lower, link_inv = blocked_cholesky(link_system)
    link_step = backward_solve(
        link_lower, link_inv, forward_solve(link_lower, link_inv, right_side[:, None])
    )[:, 0]
    newton_step = step_vec - jnp.dot(step_cols, link_step, precision=highest)
    return (newton_step[None, None], link_step)


def solution(mesh):
    return jax.shard_map(
        on_device,
        mesh=mesh,
        in_specs=(
            P("line", None, None),
            P(("scen", "line"), "tm", None),
            P(("scen", "line"), "tm", None, None),
            P(("scen", "line"), "tm", None),
            P(("scen", "line"), "tm", None),
            P(("scen", "line"), "tm", None, None),
            P(),
            P(),
            P(),
        ),
        out_specs=(P(("scen", "line"), "tm", None), P()),
        check_vma=False,
    )
```
